32 devices in a mesh: section: 2 (over x), dp: 16 (over z, y, core).
Axes of the slice: x: 2, y: 2, z: 4, core: 2. Of those that a mesh axis runs over, the one named last changes fastest.
Arguments:
- hidden_states: bfloat16 [2, 2048, 6144], P('section', 'dp'), may hold values from -27 to 27
- norm_gain: bfloat16 [2, 6144], P('section'), may hold values from 0.099609375 to 1.8984375
- gate_weight: bfloat16 [2, 6144, 32768], P('section', None, 'dp'), may hold values from -0.078125 to 0.078125
- up_weight: bfloat16 [2, 6144, 32768], P('section', None, 'dp'), may hold values from -0.078125 to 0.078125
- down_weight: bfloat16 [2, 32768, 6144], P('section', 'dp'), may hold values from -0.1875 to 0.1875
- route_rows: int32 [2, 16, 2, 16], P('section', 'dp'), may hold values from 0 to 127, as said below
- route_count: int32 [2, 16, 2], P('section', 'dp'), may hold values from 4 to 16, as said below
- route_gate: float32 [2, 16, 2, 16], P('section', 'dp'), may hold values from 0.2 to 1
Outputs:
- handed: bfloat16 [2, 2048, 6144], P('section', 'dp')
The draws below stay inside these ranges and needn't reach their ends.
Inputs may be any that keep to these rules, and one draw needn't show every extreme that they name: `route_rows`: within one section, rank and expert the 16 numbers are distinct rows of that rank's micro-batch; only the first route_count of them are live. `route_count`: in every section one of the 2 experts receives 16 live rows from every rank.
All inputs are finite; a program needn't handle non-finite values.
Results may differ from the reference program's by a relative error of at most 0.0034.
Values may be sent and summed in bfloat16 or wider, within the bound.
No kernel may reach another device: no remote copies, remote signals or barrier semaphores. Data moves between devices by JAX's collectives and lax.ppermute only.
A program may use at most 192 MiB of HBM per device.

```python
import math
import jax
import jax.numpy as jnp
from jax import lax

D = 6144
FF = 16384
E_WIN = 2
CAP = 16
TOK_DEV = 128
SECTIONS = 2
RANKS = 16
OWNERS = 8
FF_DEV = 2048
TOKENS = 2048


def draw_hidden_states(key, part):
    row_key, col_key, base_key = jax.random.split(key, 3)
    row_scale = jnp.exp(jax.random.uniform(row_key, (SECTIONS, TOKENS, 1), jnp.float32, math.log(0.3), math.log(3.0)))
    col_scale = jnp.exp(jax.random.uniform(col_key, (SECTIONS, 1, D), jnp.float32, math.log(0.3), math.log(3.0)))
    values = jax.random.truncated_normal(base_key, -3.0, 3.0, (SECTIONS, TOKENS, D), jnp.float32)
    return (values * row_scale * col_scale).astype(jnp.bfloat16)


def draw_route_rows(key, part):
    keys = jax.random.split(key, SECTIONS * RANKS * E_WIN)
    picks = jax.vmap(lambda one_key: jax.random.permutation(one_key, TOK_DEV)[:CAP])(keys)
    return picks.reshape(SECTIONS, RANKS, E_WIN, CAP).astype(jnp.int32)


def draw_route_count(key, part):
    busy_key, other_key = jax.random.split(key, 2)
    busy = jax.random.randint(busy_key, (SECTIONS, 1, 1), 0, E_WIN)
    others = jax.random.randint(other_key, (SECTIONS, RANKS, E_WIN), CAP // 4, CAP + 1)
    return jnp.where(jnp.arange(E_WIN)[None, None, :] == busy, CAP, others).astype(jnp.int32)


def levels(own_key, extent, cuts, smallest, top_value):
    gain = 1.0
    for position, blocks in cuts:
        draws = jax.random.uniform(jax.random.fold_in(jax.random.fold_in(own_key, 6), position), (blocks,), jnp.float32, smallest / len(cuts), top_value / len(cuts))
        gain = gain * jnp.repeat(jnp.exp(draws), extent[position] // blocks).reshape((-1,) + (1,) * (len(extent) - 1 - position))
    return gain


def gaussian(key, extent, deviation, limit, pieces=(), kind=jnp.bfloat16):
    entries = deviation * jax.random.normal(key, extent, jnp.float32)
    if pieces:
        entries = entries * levels(key, extent, pieces, -0.22, 0.18)
    return jnp.clip(entries, -limit, limit).astype(kind)


def setup_inputs(seed: int = 0) -> dict:
    key_list = jax.random.split(jax.random.key(seed), 9)
    hidden_states = draw_hidden_states(jax.random.fold_in(key_list[8], 71), 0)
    norm_gain = jnp.clip(1.0 + 0.18 * jax.random.normal(key_list[1], (SECTIONS, D), jnp.float32), 0.099609375, 1.8984375).astype(jnp.bfloat16)
    gate_weight = gaussian(key_list[2], (SECTIONS, D, E_WIN * FF), D ** -0.5, 0.078125, ((0, 2), (2, 16)))
    up_weight = gaussian(key_list[3], (SECTIONS, D, E_WIN * FF), D ** -0.5, 0.078125, ((0, 2), (2, 16)))
    down_weight = gaussian(key_list[4], (SECTIONS, E_WIN * FF, D), (FF // 16) ** -0.5, 0.1875, ((0, 2), (1, 16)))
    route_rows = draw_route_rows(jax.random.fold_in(key_list[8], 71), 0)
    route_count = draw_route_count(jax.random.fold_in(key_list[8], 71), 0)
    route_gate = jnp.clip(jnp.exp(math.log(1.0) - 1.609438 * jax.random.uniform(key_list[7], (SECTIONS, RANKS, E_WIN, CAP), jnp.float32) ** levels(key_list[7], (SECTIONS, RANKS, E_WIN, CAP), ((0, 2), (1, 16)), -0.2, 0.2)), 0.2, 1.0)
    return dict(hidden_states=hidden_states, norm_gain=norm_gain, gate_weight=gate_weight, up_weight=up_weight, down_weight=down_weight, route_rows=route_rows, route_count=route_count, route_gate=route_gate)


def reference(hidden_states, norm_gain, gate_weight, up_weight, down_weight, route_rows, route_count, route_gate):
    results = []
    for section_idx in range(SECTIONS):
        states = hidden_states[section_idx].astype(jnp.float32)
        normed = (states * lax.rsqrt(lax.optimization_barrier(jnp.mean(states * states, axis=-1, keepdims=True)) + 1e-05) * norm_gain[section_idx].astype(jnp.float32)).astype(jnp.bfloat16)
        blocks = normed.reshape(RANKS, TOK_DEV, D)
        picked = jax.vmap(lambda block, picks: jnp.take(block, picks, axis=0))(blocks, route_rows[section_idx])
        branch = jnp.zeros((RANKS, TOK_DEV, D), jnp.float32)
        for expert in range(E_WIN):
            flat_rows = picked[:, expert].reshape(RANKS * CAP, D)

            def add_owner(total, owner_idx):
                start = (expert * OWNERS + owner_idx) * FF_DEV
                gate_cols = lax.dynamic_slice_in_dim(gate_weight[section_idx], start, FF_DEV, 1)
                up_cols = lax.dynamic_slice_in_dim(up_weight[section_idx], start, FF_DEV, 1)
                down_rows = lax.dynamic_slice_in_dim(down_weight[section_idx], start, FF_DEV, 0)
                gate_part = jnp.dot(flat_rows, gate_cols, preferred_element_type=jnp.float32)
                up_part = jnp.dot(flat_rows, up_cols, preferred_element_type=jnp.float32)
                activated = (jax.nn.silu(gate_part) * up_part).astype(jnp.bfloat16)
                partial_out = jnp.dot(activated, down_rows, preferred_element_type=jnp.float32).astype(jnp.bfloat16)
                return (total + partial_out.astype(jnp.float32), None)
            total, _ = lax.scan(add_owner, jnp.zeros((RANKS * CAP, D), jnp.float32), jnp.arange(OWNERS, dtype=jnp.int32))
            summed = total.reshape(RANKS, CAP, D)
            live_mask = jnp.arange(CAP)[None, :] < route_count[section_idx][:, expert][:, None]
            weighting = jnp.where(live_mask, route_gate[section_idx][:, expert], 0.0)
            contrib = weighting[..., None] * summed
            branch = jax.vmap(lambda acc, picks, values: acc.at[picks].add(values))(branch, route_rows[section_idx][:, expert], contrib)
        results.append((states + branch.reshape(TOKENS, D)).astype(jnp.bfloat16))
    layer_out = jnp.stack(results)
    return jnp.roll(layer_out, 1, axis=0)
```

```python
import jax
import jax.numpy as jnp
from jax import lax
from jax.sharding import Mesh, PartitionSpec as P


def shifted(block, axes, size, distance):
    route = [(i, (i + distance) % size) for i in range(size)]
    return lax.ppermute(block, axes, route)


def body(
    hidden_states,
    norm_gain,
    gate_weight,
    up_weight,
    down_weight,
    route_rows,
    route_count,
    route_gate,
):
    states = hidden_states[0]
    scale_gain = norm_gain[0]
    gate_cols = gate_weight[0]
    up_cols = up_weight[0]
    down_rows = down_weight[0]
    slot_rows = route_rows[0, 0]
    live_count = route_count[0, 0]
    slot_gates = route_gate[0, 0]
    tok_count, width = states.shape
    experts, capacity = slot_rows.shape
    sections = lax.axis_size("section")
    n_ex = lax.axis_size("ex")
    n_chip = lax.axis_size("chip")
    n_core = lax.axis_size("core")
    ex_me = lax.axis_index("ex")
    core_me = lax.axis_index("core")

    live_mask = jnp.arange(capacity)[None, :] < live_count[:, None]
    weighting = jnp.where(live_mask, slot_gates, 0.0)
    states_in = shifted(states, "section", sections, 1)
    rows_in = shifted(slot_rows, "section", sections, 1)
    weights_in = shifted(weighting, "section", sections, 1)

    chosen = jnp.take(states, slot_rows.reshape(-1), axis=0).astype(jnp.float32)
    normed = (
        chosen
        * lax.rsqrt(jnp.mean(chosen * chosen, axis=-1, keepdims=True) + 1e-05)
        * scale_gain.astype(jnp.float32)
    ).astype(jnp.bfloat16)
    picked = normed.reshape(experts, capacity, width)

    parts = [lax.dynamic_index_in_dim(picked, ex_me, 0, keepdims=False)]
    for k in range(1, n_ex):
        outgoing = lax.dynamic_index_in_dim(picked, (ex_me + k) % n_ex, 0, keepdims=False)
        parts.append(shifted(outgoing, "ex", n_ex, k))
    block = jnp.stack(parts)
    gathered = lax.all_gather(block, "chip", axis=0, tiled=False)
    gathered = lax.all_gather(gathered, "core", axis=0, tiled=False)
    flat_rows = gathered.reshape(-1, width)

    gate_part = jnp.dot(flat_rows, gate_cols, preferred_element_type=jnp.float32)
    up_part = jnp.dot(flat_rows, up_cols, preferred_element_type=jnp.float32)
    activated = (jax.nn.silu(gate_part) * up_part).astype(jnp.bfloat16)
    partial_out = jnp.dot(activated, down_rows, preferred_element_type=jnp.float32).astype(
        jnp.bfloat16
    )
    partials = partial_out.reshape(gathered.shape)

    summed = lax.dynamic_index_in_dim(partials, core_me, 0, keepdims=False).astype(jnp.float32)
    for k in range(1, n_core):
        outgoing = lax.dynamic_index_in_dim(partials, (core_me + k) % n_core, 0, keepdims=False)
        summed = summed + shifted(outgoing, "core", n_core, k).astype(jnp.float32)
    reduced = lax.psum_scatter(summed, "chip", scatter_dimension=0, tiled=False)

    got = []
    for k in range(n_ex):
        if k == 0:
            got.append(shifted(reduced[0], "section", sections, 1))
        else:
            route = []
            for s in range(sections):
                for e in range(n_ex):
                    route.append((s * n_ex + e, ((s + 1) % sections) * n_ex + (e - k) % n_ex))
            got.append(lax.ppermute(reduced[k], ("section", "ex"), route))
    stacked = jnp.stack(got)
    order = (ex_me + jnp.arange(n_ex)) % n_ex
    expert_out = jnp.zeros_like(stacked).at[order].set(stacked)

    one_hot = (rows_in[..., None] == jnp.arange(tok_count)[None, None, :]).astype(
        jnp.float32
    ) * weights_in[..., None]
    branch = jnp.einsum("ect,ecd->td", one_hot, expert_out, precision=lax.Precision.HIGHEST)
    layer_out = (states_in.astype(jnp.float32) + branch).astype(jnp.bfloat16)
    return layer_out[None]


def solution(mesh):
    def run(*args):
        experts = args[5].shape[2]
        sections, ranks = mesh.devices.shape
        owners = ranks // experts
        cores = 2 if owners % 2 == 0 else 1
        devices = mesh.devices.reshape(sections, experts, owners // cores, cores)
        fine = Mesh(devices, ("section", "ex", "chip", "core"))
        dp = ("ex", "chip", "core")
        placed = (
            P("section", dp, None),
            P("section", None),
            P("section", None, dp),
            P("section", None, dp),
            P("section", dp, None),
            P("section", dp, None, None),
            P("section", dp, None),
            P("section", dp, None, None),
        )
        return jax.shard_map(
            body, mesh=fine, in_specs=placed, out_specs=P("section", dp, None), check_vma=False
        )(*args)

    return run
```

```python
import jax
import jax.numpy as jnp
from jax import lax
from jax.sharding import Mesh, PartitionSpec as P

CHIP_SUM_DTYPE = jnp.float32
HAND_DTYPE = jnp.float32


def shifted(block, axes, size, distance):
    route = [(i, (i + distance) % size) for i in range(size)]
    return lax.ppermute(block, axes, route)


def partnered(block, axes, size, step):
    if size & (size - 1) == 0:
        route = [(i, i ^ step) for i in range(size)]
    else:
        route = [(i, (i + step) % size) for i in range(size)]
    return lax.ppermute(block, axes, route)


def back_partnered(block, axes, size, step):
    if size & (size - 1) == 0:
        route = [(i, i ^ step) for i in range(size)]
    else:
        route = [(i, (i - step) % size) for i in range(size)]
    return lax.ppermute(block, axes, route)


def body(
    hidden_states,
    norm_gain,
    gate_weight,
    up_weight,
    down_weight,
    route_rows,
    route_count,
    route_gate,
):
    states = hidden_states[0]
    scale_gain = norm_gain[0]
    gate_cols = gate_weight[0]
    up_cols = up_weight[0]
    down_rows = down_weight[0]
    slot_rows = route_rows[0, 0]
    live_count = route_count[0, 0]
    slot_gates = route_gate[0, 0]
    tok_count, width = states.shape
    experts, capacity = slot_rows.shape
    sections = lax.axis_size("section")
    n_ex = lax.axis_size("ex")
    n_chip = lax.axis_size("chip")
    n_core = lax.axis_size("core")
    ex_me = lax.axis_index("ex")

    live_mask = jnp.arange(capacity)[None, :] < live_count[:, None]
    weighting = jnp.where(live_mask, slot_gates, 0.0)
    states_in = shifted(states, "section", sections, 1)
    rows_in = shifted(slot_rows, "section", sections, 1)
    weights_in = shifted(weighting, "section", sections, 1)

    chosen = jnp.take(states, slot_rows.reshape(-1), axis=0).astype(jnp.float32)
    normed = (
        chosen
        * lax.rsqrt(jnp.mean(chosen * chosen, axis=-1, keepdims=True) + 1e-05)
        * scale_gain.astype(jnp.float32)
    ).astype(jnp.bfloat16)
    picked = normed.reshape(experts, capacity, width)

    parts = [lax.dynamic_index_in_dim(picked, ex_me, 0, keepdims=False)]
    for k in range(1, n_ex):
        outgoing = lax.dynamic_index_in_dim(picked, (ex_me + k) % n_ex, 0, keepdims=False)
        parts.append(shifted(outgoing, "ex", n_ex, k))
    block = jnp.stack(parts)
    chip_rows = [block] + [partnered(block, "chip", n_chip, m) for m in range(1, n_chip)]
    chip_rows = jnp.stack(chip_rows)
    core_rows = [chip_rows] + [partnered(chip_rows, "core", n_core, q) for q in range(1, n_core)]
    gathered = jnp.stack(core_rows)
    flat_rows = gathered.reshape(-1, width)

    gate_part = jnp.dot(flat_rows, gate_cols, preferred_element_type=jnp.float32)
    up_part = jnp.dot(flat_rows, up_cols, preferred_element_type=jnp.float32)
    activated = (jax.nn.silu(gate_part) * up_part).astype(jnp.bfloat16)
    partial_out = jnp.dot(activated, down_rows, preferred_element_type=jnp.float32).astype(
        jnp.bfloat16
    )
    partials = partial_out.reshape(gathered.shape)

    summed = partials[0].astype(jnp.float32)
    for q in range(1, n_core):
        summed = summed + back_partnered(partials[q], "core", n_core, q).astype(jnp.float32)
    reduced = summed[0]
    for m in range(1, n_chip):
        sent = back_partnered(summed[m].astype(CHIP_SUM_DTYPE), "chip", n_chip, m)
        reduced = reduced + sent.astype(jnp.float32)

    got = []
    for k in range(n_ex):
        outgoing = reduced[k].astype(HAND_DTYPE)
        if k == 0:
            got.append(shifted(outgoing, "section", sections, 1))
        else:
            route = []
            for s in range(sections):
                for e in range(n_ex):
                    route.append((s * n_ex + e, ((s + 1) % sections) * n_ex + (e - k) % n_ex))
            got.append(lax.ppermute(outgoing, ("section", "ex"), route))
    stacked = jnp.stack(got).astype(jnp.float32)
    order = (ex_me + jnp.arange(n_ex)) % n_ex
    expert_out = jnp.zeros_like(stacked).at[order].set(stacked)

    one_hot = (rows_in[..., None] == jnp.arange(tok_count)[None, None, :]).astype(
        jnp.float32
    ) * weights_in[..., None]
    branch = jnp.einsum("ect,ecd->td", one_hot, expert_out, precision=lax.Precision.HIGHEST)
    layer_out = (states_in.astype(jnp.float32) + branch).astype(jnp.bfloat16)
    return layer_out[None]


def solution(mesh):
    def run(*args):
        experts = args[5].shape[2]
        sections, ranks = mesh.devices.shape
        owners = ranks // experts
        cores = 2 if owners % 2 == 0 else 1
        devices = mesh.devices.reshape(sections, experts, owners // cores, cores)
        fine = Mesh(devices, ("section", "ex", "chip", "core"))
        dp = ("ex", "chip", "core")
        placed = (
            P("section", dp, None),
            P("section", None),
            P("section", None, dp),
            P("section", None, dp),
            P("section", dp, None),
            P("section", dp, None, None),
            P("section", dp, None),
            P("section", dp, None, None),
        )
        return jax.shard_map(
            body, mesh=fine, in_specs=placed, out_specs=P("section", dp, None), check_vma=False
        )(*args)

    return run
```

```python
import jax
import jax.numpy as jnp
from jax import lax
from jax.sharding import Mesh, PartitionSpec as P

CHIP_SUM_DTYPE = jnp.bfloat16
HAND_DTYPE = jnp.bfloat16


def shifted(block, axes, size, distance):
    route = [(i, (i + distance) % size) for i in range(size)]
    return lax.ppermute(block, axes, route)


def partnered(block, axes, size, step):
    if size & (size - 1) == 0:
        route = [(i, i ^ step) for i in range(size)]
    else:
        route = [(i, (i + step) % size) for i in range(size)]
    return lax.ppermute(block, axes, route)


def back_partnered(block, axes, size, step):
    if size & (size - 1) == 0:
        route = [(i, i ^ step) for i in range(size)]
    else:
        route = [(i, (i - step) % size) for i in range(size)]
    return lax.ppermute(block, axes, route)


def body(
    hidden_states,
    norm_gain,
    gate_weight,
    up_weight,
    down_weight,
    route_rows,
    route_count,
    route_gate,
):
    states = hidden_states[0]
    scale_gain = norm_gain[0]
    gate_cols = gate_weight[0]
    up_cols = up_weight[0]
    down_rows = down_weight[0]
    slot_rows = route_rows[0, 0]
    live_count = route_count[0, 0]
    slot_gates = route_gate[0, 0]
    tok_count, width = states.shape
    experts, capacity = slot_rows.shape
    sections = lax.axis_size("section")
    n_ex = lax.axis_size("ex")
    n_chip = lax.axis_size("chip")
    n_core = lax.axis_size("core")
    ex_me = lax.axis_index("ex")

    live_mask = jnp.arange(capacity)[None, :] < live_count[:, None]
    weighting = jnp.where(live_mask, slot_gates, 0.0)
    states_in = shifted(states, "section", sections, 1)
    rows_in = shifted(slot_rows, "section", sections, 1)
    weights_in = shifted(weighting, "section", sections, 1)

    selector = (slot_rows.reshape(-1)[:, None] == jnp.arange(tok_count)[None, :]).astype(states.dtype)
    chosen = jnp.dot(selector, states, preferred_element_type=jnp.float32)
    normed = (
        chosen
        * lax.rsqrt(jnp.mean(chosen * chosen, axis=-1, keepdims=True) + 1e-05)
        * scale_gain.astype(jnp.float32)
    ).astype(jnp.bfloat16)
    picked = normed.reshape(experts, capacity, width)

    parts = [lax.dynamic_index_in_dim(picked, ex_me, 0, keepdims=False)]
    for k in range(1, n_ex):
        outgoing = lax.dynamic_index_in_dim(picked, (ex_me + k) % n_ex, 0, keepdims=False)
        parts.append(shifted(outgoing, "ex", n_ex, k))
    chip_rows = [parts] + [
        [partnered(part, "chip", n_chip, m) for part in parts] for m in range(1, n_chip)
    ]
    chip_rows = [jnp.stack([chip_rows[m][k] for m in range(n_chip)]) for k in range(n_ex)]
    core_rows = [chip_rows] + [
        [partnered(rows, "core", n_core, q) for rows in chip_rows] for q in range(1, n_core)
    ]
    gathered = jnp.stack([jnp.stack(core_rows[q], axis=1) for q in range(n_core)])
    flat_rows = gathered.reshape(-1, width)

    gate_part = jnp.dot(flat_rows, gate_cols, preferred_element_type=jnp.float32)
    up_part = jnp.dot(flat_rows, up_cols, preferred_element_type=jnp.float32)
    activated = (jax.nn.silu(gate_part) * up_part).astype(jnp.bfloat16)
    partial_out = jnp.dot(activated, down_rows, preferred_element_type=jnp.float32).astype(
        jnp.bfloat16
    )
    partials = partial_out.reshape(gathered.shape)

    summed = partials[0].astype(jnp.float32)
    for q in range(1, n_core):
        summed = summed + back_partnered(partials[q], "core", n_core, q).astype(jnp.float32)
    reduced = summed[0]
    for m in range(1, n_chip):
        sent = back_partnered(summed[m].astype(CHIP_SUM_DTYPE), "chip", n_chip, m)
        reduced = reduced + sent.astype(jnp.float32)

    got = []
    for k in range(n_ex):
        outgoing = reduced[k].astype(HAND_DTYPE)
        if k == 0:
            got.append(shifted(outgoing, "section", sections, 1))
        else:
            route = []
            for s in range(sections):
                for e in range(n_ex):
                    route.append((s * n_ex + e, ((s + 1) % sections) * n_ex + (e - k) % n_ex))
            got.append(lax.ppermute(outgoing, ("section", "ex"), route))
    stacked = jnp.stack(got).astype(jnp.float32)
    order = (ex_me + jnp.arange(n_ex)) % n_ex
    expert_out = jnp.zeros_like(stacked).at[order].set(stacked)

    one_hot = (rows_in[..., None] == jnp.arange(tok_count)[None, None, :]).astype(
        jnp.float32
    ) * weights_in[..., None]
    branch = jnp.einsum("ect,ecd->td", one_hot, expert_out, precision=lax.Precision.HIGHEST)
    layer_out = (states_in.astype(jnp.float32) + branch).astype(jnp.bfloat16)
    return layer_out[None]


def solution(mesh):
    def run(*args):
        experts = args[5].shape[2]
        sections, ranks = mesh.devices.shape
        owners = ranks // experts
        cores = 2 if owners % 2 == 0 else 1
        devices = mesh.devices.reshape(sections, experts, owners // cores, cores)
        fine = Mesh(devices, ("section", "ex", "chip", "core"))
        dp = ("ex", "chip", "core")
        placed = (
            P("section", dp, None),
            P("section", None),
            P("section", None, dp),
            P("section", None, dp),
            P("section", dp, None),
            P("section", dp, None, None),
            P("section", dp, None),
            P("section", dp, None, None),
        )
        return jax.shard_map(
            body, mesh=fine, in_specs=placed, out_specs=P("section", dp, None), check_vma=False
        )(*args)

    return run
```

```python
import jax
import jax.numpy as jnp
from jax import lax
from jax.sharding import Mesh, PartitionSpec as P

CHIP_SUM_DTYPE = jnp.bfloat16
HAND_DTYPE = jnp.bfloat16


def shifted(block, axes, size, distance):
    route = [(i, (i + distance) % size) for i in range(size)]
    return lax.ppermute(block, axes, route)


def partnered(block, axes, size, step):
    if size & (size - 1) == 0:
        route = [(i, i ^ step) for i in range(size)]
    else:
        route = [(i, (i + step) % size) for i in range(size)]
    return lax.ppermute(block, axes, route)


def back_partnered(block, axes, size, step):
    if size & (size - 1) == 0:
        route = [(i, i ^ step) for i in range(size)]
    else:
        route = [(i, (i - step) % size) for i in range(size)]
    return lax.ppermute(block, axes, route)


def body(
    hidden_states,
    norm_gain,
    gate_weight,
    up_weight,
    down_weight,
    route_rows,
    route_count,
    route_gate,
):
    states = hidden_states[0]
    scale_gain = norm_gain[0]
    gate_cols = gate_weight[0]
    up_cols = up_weight[0]
    down_rows = down_weight[0]
    slot_rows = route_rows[0, 0]
    live_count = route_count[0, 0]
    slot_gates = route_gate[0, 0]
    tok_count, width = states.shape
    experts, capacity = slot_rows.shape
    sections = lax.axis_size("section")
    n_ex = lax.axis_size("ex")
    n_chip = lax.axis_size("chip")
    n_core = lax.axis_size("core")
    ex_me = lax.axis_index("ex")

    live_mask = jnp.arange(capacity)[None, :] < live_count[:, None]
    weighting = jnp.where(live_mask, slot_gates, 0.0)
    states_in = shifted(states, "section", sections, 1)
    rows_in = shifted(slot_rows, "section", sections, 1)
    weights_in = shifted(weighting, "section", sections, 1)

    selector = (slot_rows.reshape(-1)[:, None] == jnp.arange(tok_count)[None, :]).astype(states.dtype)
    chosen = jnp.dot(selector, states, preferred_element_type=jnp.float32)
    normed = (
        chosen
        * lax.rsqrt(jnp.mean(chosen * chosen, axis=-1, keepdims=True) + 1e-05)
        * scale_gain.astype(jnp.float32)
    ).astype(jnp.bfloat16)
    picked = normed.reshape(experts, capacity, width)

    parts = [lax.dynamic_index_in_dim(picked, ex_me, 0, keepdims=False)]
    for k in range(1, n_ex):
        outgoing = lax.dynamic_index_in_dim(picked, (ex_me + k) % n_ex, 0, keepdims=False)
        parts.append(shifted(outgoing, "ex", n_ex, k))
    chip_rows = [parts] + [
        [partnered(part, "chip", n_chip, m) for part in parts] for m in range(1, n_chip)
    ]
    chip_rows = [jnp.stack([chip_rows[m][k] for m in range(n_chip)]) for k in range(n_ex)]
    core_rows = [chip_rows] + [
        [partnered(rows, "core", n_core, q) for rows in chip_rows] for q in range(1, n_core)
    ]
    gathered = jnp.stack([jnp.stack(core_rows[q], axis=1) for q in range(n_core)])
    flat_rows = gathered.reshape(-1, width)

    gate_part = jnp.dot(flat_rows, gate_cols, preferred_element_type=jnp.float32)
    up_part = jnp.dot(flat_rows, up_cols, preferred_element_type=jnp.float32)
    activated = (jax.nn.silu(gate_part) * up_part).astype(jnp.bfloat16)
    partial_out = jnp.dot(activated, down_rows, preferred_element_type=jnp.float32).astype(
        jnp.bfloat16
    )
    states_in, rows_in, weights_in, partial_out = lax.optimization_barrier(
        (states_in, rows_in, weights_in, partial_out)
    )
    partials = partial_out.reshape(gathered.shape)

    summed = partials[0].astype(jnp.float32)
    for q in range(1, n_core):
        summed = summed + back_partnered(partials[q], "core", n_core, q).astype(jnp.float32)
    reduced = summed[0]
    for m in range(1, n_chip):
        sent = back_partnered(summed[m].astype(CHIP_SUM_DTYPE), "chip", n_chip, m)
        reduced = reduced + sent.astype(jnp.float32)

    got = []
    for k in range(n_ex):
        outgoing = reduced[k].astype(HAND_DTYPE)
        if k == 0:
            got.append(shifted(outgoing, "section", sections, 1))
        else:
            route = []
            for s in range(sections):
                for e in range(n_ex):
                    route.append((s * n_ex + e, ((s + 1) % sections) * n_ex + (e - k) % n_ex))
            got.append(lax.ppermute(outgoing, ("section", "ex"), route))
    stacked = jnp.stack(got).astype(jnp.float32)
    order = (ex_me + jnp.arange(n_ex)) % n_ex
    expert_out = jnp.zeros_like(stacked).at[order].set(stacked)

    one_hot = (rows_in[..., None] == jnp.arange(tok_count)[None, None, :]).astype(
        jnp.float32
    ) * weights_in[..., None]
    branch = jnp.einsum("ect,ecd->td", one_hot, expert_out, precision=lax.Precision.HIGHEST)
    layer_out = (states_in.astype(jnp.float32) + branch).astype(jnp.bfloat16)
    return layer_out[None]


def solution(mesh):
    def run(*args):
        experts = args[5].shape[2]
        sections, ranks = mesh.devices.shape
        owners = ranks // experts
        cores = 2 if owners % 2 == 0 else 1
        devices = mesh.devices.reshape(sections, experts, owners // cores, cores)
        fine = Mesh(devices, ("section", "ex", "chip", "core"))
        dp = ("ex", "chip", "core")
        placed = (
            P("section", dp, None),
            P("section", None),
            P("section", None, dp),
            P("section", None, dp),
            P("section", dp, None),
            P("section", dp, None, None),
            P("section", dp, None),
            P("section", dp, None, None),
        )
        return jax.shard_map(
            body, mesh=fine, in_specs=placed, out_specs=P("section", dp, None), check_vma=False
        )(*args)

    return run
```

```python
import jax
import jax.numpy as jnp
from jax import lax
from jax.sharding import Mesh, PartitionSpec as P

SUM_DTYPE = jnp.bfloat16


def shifted(block, axes, size, distance):
    route = [(i, (i + distance) % size) for i in range(size)]
    return lax.ppermute(block, axes, route)


def chip_route(n_chip, n_core, stage, levels):
    route = []
    for k in range(n_chip):
        for c in range(n_core):
            bit = (stage + c) % levels
            route.append((k * n_core + c, (k ^ (1 << bit)) * n_core + c))
    return route


def body(
    hidden_states,
    norm_gain,
    gate_weight,
    up_weight,
    down_weight,
    route_rows,
    route_count,
    route_gate,
):
    states = hidden_states[0]
    scale_gain = norm_gain[0]
    gate_cols = gate_weight[0]
    up_cols = up_weight[0]
    down_rows = down_weight[0]
    slot_rows = route_rows[0, 0]
    live_count = route_count[0, 0]
    slot_gates = route_gate[0, 0]
    tok_count, width = states.shape
    experts, capacity = slot_rows.shape
    sections = lax.axis_size("section")
    n_ex = lax.axis_size("ex")
    n_chip = lax.axis_size("chip")
    n_core = lax.axis_size("core")
    levels = n_chip.bit_length() - 1
    ex_me = lax.axis_index("ex")

    live_mask = jnp.arange(capacity)[None, :] < live_count[:, None]
    weighting = jnp.where(live_mask, slot_gates, 0.0)
    selector_out = (slot_rows[..., None] == jnp.arange(tok_count)[None, None, :]).astype(
        jnp.float32
    ) * weighting[..., None]
    states_in = shifted(states, "section", sections, 1)
    selector_in = shifted(selector_out, "section", sections, 1)

    selector = (slot_rows.reshape(-1)[:, None] == jnp.arange(tok_count)[None, :]).astype(states.dtype)
    chosen = jnp.dot(selector, states, preferred_element_type=jnp.float32)
    normed = (
        chosen
        * lax.rsqrt(jnp.mean(chosen * chosen, axis=-1, keepdims=True) + 1e-05)
        * scale_gain.astype(jnp.float32)
    ).astype(jnp.bfloat16)
    picked = normed.reshape(experts, capacity, width)

    parts = [lax.dynamic_index_in_dim(picked, ex_me, 0, keepdims=False)]
    for k in range(1, n_ex):
        outgoing = lax.dynamic_index_in_dim(picked, (ex_me + k) % n_ex, 0, keepdims=False)
        parts.append(shifted(outgoing, "ex", n_ex, k))
    chip_rows = []
    for part in parts:
        held = part[None]
        for stage in range(levels):
            arrived = lax.ppermute(held, ("chip", "core"), chip_route(n_chip, n_core, stage, levels))
            held = jnp.concatenate([held, arrived])
        chip_rows.append(held)
    core_rows = [chip_rows] + [
        [shifted(rows, "core", n_core, q) for rows in chip_rows] for q in range(1, n_core)
    ]
    gathered = jnp.stack([jnp.stack(core_rows[q], axis=1) for q in range(n_core)])
    flat_rows = gathered.reshape(-1, width)

    gate_part = jnp.dot(flat_rows, gate_cols, preferred_element_type=jnp.float32)
    up_part = jnp.dot(flat_rows, up_cols, preferred_element_type=jnp.float32)
    activated = (jax.nn.silu(gate_part) * up_part).astype(jnp.bfloat16)
    partial_out = jnp.dot(activated, down_rows, preferred_element_type=jnp.float32).astype(
        jnp.bfloat16
    )
    states_in, selector_in, partial_out = lax.optimization_barrier(
        (states_in, selector_in, partial_out)
    )
    partials = partial_out.reshape(gathered.shape)

    summed = partials[0].astype(jnp.float32)
    for q in range(1, n_core):
        summed = summed + shifted(partials[q], "core", n_core, -q).astype(jnp.float32)
    for stage in reversed(range(levels)):
        half = summed.shape[0] // 2
        sent = summed[half:].astype(SUM_DTYPE)
        arrived = lax.ppermute(sent, ("chip", "core"), chip_route(n_chip, n_core, stage, levels))
        summed = summed[:half] + arrived.astype(jnp.float32)
    reduced = summed[0]

    got = []
    for k in range(n_ex):
        outgoing = reduced[k].astype(SUM_DTYPE)
        if k == 0:
            got.append(shifted(outgoing, "section", sections, 1))
        else:
            route = []
            for s in range(sections):
                for e in range(n_ex):
                    route.append((s * n_ex + e, ((s + 1) % sections) * n_ex + (e - k) % n_ex))
            got.append(lax.ppermute(outgoing, ("section", "ex"), route))
    stacked = jnp.stack(got).astype(jnp.float32)
    order = (ex_me + jnp.arange(n_ex)) % n_ex
    expert_out = jnp.zeros_like(stacked).at[order].set(stacked)

    branch = jnp.einsum("ect,ecd->td", selector_in, expert_out, precision=lax.Precision.HIGHEST)
    layer_out = (states_in.astype(jnp.float32) + branch).astype(jnp.bfloat16)
    return layer_out[None]


def solution(mesh):
    def run(*args):
        experts = args[5].shape[2]
        sections, ranks = mesh.devices.shape
        owners = ranks // experts
        cores = 2 if owners % 2 == 0 else 1
        devices = mesh.devices.reshape(sections, experts, owners // cores, cores)
        fine = Mesh(devices, ("section", "ex", "chip", "core"))
        dp = ("ex", "chip", "core")
        placed = (
            P("section", dp, None),
            P("section", None),
            P("section", None, dp),
            P("section", None, dp),
            P("section", dp, None),
            P("section", dp, None, None),
            P("section", dp, None),
            P("section", dp, None, None),
        )
        return jax.shard_map(
            body, mesh=fine, in_specs=placed, out_specs=P("section", dp, None), check_vma=False
        )(*args)

    return run
```

```python
import jax
import jax.numpy as jnp
from jax import lax
from jax.sharding import Mesh, PartitionSpec as P

SUM_DTYPE = jnp.bfloat16
PIECES = 2


def shifted(block, axes, size, distance):
    route = [(i, (i + distance) % size) for i in range(size)]
    return lax.ppermute(block, axes, route)


def chip_route(n_chip, n_core, stage, levels):
    route = []
    for k in range(n_chip):
        for c in range(n_core):
            bit = (stage + c) % levels
            route.append((k * n_core + c, (k ^ (1 << bit)) * n_core + c))
    return route


def body(
    hidden_states,
    norm_gain,
    gate_weight,
    up_weight,
    down_weight,
    route_rows,
    route_count,
    route_gate,
):
    states = hidden_states[0]
    scale_gain = norm_gain[0]
    gate_cols = gate_weight[0]
    up_cols = up_weight[0]
    down_rows = down_weight[0]
    slot_rows = route_rows[0, 0]
    live_count = route_count[0, 0]
    slot_gates = route_gate[0, 0]
    tok_count, width = states.shape
    experts, capacity = slot_rows.shape
    sections = lax.axis_size("section")
    n_ex = lax.axis_size("ex")
    n_chip = lax.axis_size("chip")
    n_core = lax.axis_size("core")
    levels = n_chip.bit_length() - 1
    ex_me = lax.axis_index("ex")

    live_mask = jnp.arange(capacity)[None, :] < live_count[:, None]
    weighting = jnp.where(live_mask, slot_gates, 0.0)
    selector_out = (slot_rows[..., None] == jnp.arange(tok_count)[None, None, :]).astype(
        jnp.float32
    ) * weighting[..., None]
    order = (ex_me + jnp.arange(n_ex)) % n_ex
    selector_out = jnp.take(selector_out, order, axis=0)
    early_in = shifted(states[: tok_count // 2], "section", sections, 1)
    late_in = shifted(states[tok_count // 2 :], "section", sections, 1)
    selector_in = shifted(selector_out, "section", sections, 1)

    selector = (slot_rows.reshape(-1)[:, None] == jnp.arange(tok_count)[None, :]).astype(states.dtype)
    chosen = jnp.dot(selector, states, preferred_element_type=jnp.float32)
    normed = (
        chosen
        * lax.rsqrt(jnp.mean(chosen * chosen, axis=-1, keepdims=True) + 1e-05)
        * scale_gain.astype(jnp.float32)
    ).astype(jnp.bfloat16)
    picked = normed.reshape(experts, capacity, width)

    parts = [lax.dynamic_index_in_dim(picked, ex_me, 0, keepdims=False)]
    for k in range(1, n_ex):
        outgoing = lax.dynamic_index_in_dim(picked, (ex_me + k) % n_ex, 0, keepdims=False)
        parts.append(shifted(outgoing, "ex", n_ex, k))
    chip_rows = []
    for part in parts:
        held = part[None]
        for stage in range(levels):
            arrived = lax.ppermute(held, ("chip", "core"), chip_route(n_chip, n_core, stage, levels))
            held = jnp.concatenate([held, arrived])
        chip_rows.append(held)
    core_rows = [chip_rows] + [
        [shifted(rows, "core", n_core, q) for rows in chip_rows] for q in range(1, n_core)
    ]
    gathered = jnp.stack([jnp.stack(core_rows[q], axis=1) for q in range(n_core)])
    early_in, gathered = lax.optimization_barrier((early_in, gathered))
    flat_rows = gathered.reshape(-1, width)

    gate_part = jnp.dot(flat_rows, gate_cols, preferred_element_type=jnp.float32)
    up_part = jnp.dot(flat_rows, up_cols, preferred_element_type=jnp.float32)
    activated = (jax.nn.silu(gate_part) * up_part).astype(jnp.bfloat16)

    pieces = PIECES if width % (PIECES * 128) == 0 else 1
    span = width // pieces
    got = [[] for _ in range(n_ex)]
    for piece in range(pieces):
        cols = down_rows[:, piece * span:(piece + 1) * span]
        partial_out = jnp.dot(activated, cols, preferred_element_type=jnp.float32).astype(
            jnp.bfloat16
        )
        if piece == 0:
            late_in, selector_in, partial_out = lax.optimization_barrier(
                (late_in, selector_in, partial_out)
            )
        partials = partial_out.reshape(gathered.shape[:-1] + (span,))

        summed = partials[0].astype(jnp.float32)
        for q in range(1, n_core):
            summed = summed + shifted(partials[q], "core", n_core, -q).astype(jnp.float32)
        for stage in reversed(range(levels)):
            half = summed.shape[0] // 2
            sent = summed[half:].astype(SUM_DTYPE)
            arrived = lax.ppermute(sent, ("chip", "core"), chip_route(n_chip, n_core, stage, levels))
            summed = summed[:half] + arrived.astype(jnp.float32)
        reduced = summed[0]

        for k in range(n_ex):
            outgoing = reduced[k].astype(SUM_DTYPE)
            if k == 0:
                got[k].append(shifted(outgoing, "section", sections, 1))
            else:
                route = []
                for s in range(sections):
                    for e in range(n_ex):
                        route.append((s * n_ex + e, ((s + 1) % sections) * n_ex + (e - k) % n_ex))
                got[k].append(lax.ppermute(outgoing, ("section", "ex"), route))
    expert_out = jnp.stack([jnp.concatenate(pieces_k, axis=-1) for pieces_k in got])
    states_in = jnp.concatenate([early_in, late_in])

    branch = jnp.einsum(
        "ect,ecd->td", selector_in, expert_out.astype(jnp.float32), precision=lax.Precision.HIGHEST
    )
    layer_out = (states_in.astype(jnp.float32) + branch).astype(jnp.bfloat16)
    return layer_out[None]


def solution(mesh):
    def run(*args):
        experts = args[5].shape[2]
        sections, ranks = mesh.devices.shape
        owners = ranks // experts
        cores = 2 if owners % 2 == 0 else 1
        devices = mesh.devices.reshape(sections, experts, owners // cores, cores)
        fine = Mesh(devices, ("section", "ex", "chip", "core"))
        dp = ("ex", "chip", "core")
        placed = (
            P("section", dp, None),
            P("section", None),
            P("section", None, dp),
            P("section", None, dp),
            P("section", dp, None),
            P("section", dp, None, None),
            P("section", dp, None),
            P("section", dp, None, None),
        )
        return jax.shard_map(
            body, mesh=fine, in_specs=placed, out_specs=P("section", dp, None), check_vma=False
        )(*args)

    return run
```

```python
import jax
import jax.numpy as jnp
from jax import lax
from jax.sharding import Mesh, PartitionSpec as P

SUM_DTYPE = jnp.bfloat16
PIECES = 2


def shifted(block, axes, size, distance):
    route = [(i, (i + distance) % size) for i in range(size)]
    return lax.ppermute(block, axes, route)


def chip_route(n_chip, n_core, stage, levels):
    route = []
    for k in range(n_chip):
        for c in range(n_core):
            bit = (stage + c) % levels
            route.append((k * n_core + c, (k ^ (1 << bit)) * n_core + c))
    return route


def body(
    hidden_states,
    norm_gain,
    gate_weight,
    up_weight,
    down_weight,
    route_rows,
    route_count,
    route_gate,
):
    states = hidden_states[0]
    scale_gain = norm_gain[0]
    gate_cols = gate_weight[0]
    up_cols = up_weight[0]
    down_rows = down_weight[0]
    slot_rows = route_rows[0, 0]
    live_count = route_count[0, 0]
    slot_gates = route_gate[0, 0]
    tok_count, width = states.shape
    experts, capacity = slot_rows.shape
    sections = lax.axis_size("section")
    n_ex = lax.axis_size("ex")
    n_chip = lax.axis_size("chip")
    n_core = lax.axis_size("core")
    levels = n_chip.bit_length() - 1
    ex_me = lax.axis_index("ex")

    live_mask = jnp.arange(capacity)[None, :] < live_count[:, None]
    weighting = jnp.where(live_mask, slot_gates, 0.0)
    selector_out = (slot_rows[..., None] == jnp.arange(tok_count)[None, None, :]).astype(
        jnp.float32
    ) * weighting[..., None]
    order = (ex_me + jnp.arange(n_ex)) % n_ex
    selector_out = jnp.take(selector_out, order, axis=0)
    early_in = shifted(states[: tok_count // 2], "section", sections, 1)
    late_in = shifted(states[tok_count // 2 :], "section", sections, 1)
    selector_in = shifted(selector_out, "section", sections, 1)

    selector = (slot_rows.reshape(-1)[:, None] == jnp.arange(tok_count)[None, :]).astype(states.dtype)
    raw = jnp.dot(selector, states, preferred_element_type=jnp.float32).astype(states.dtype)
    raw = raw.reshape(experts, capacity, width)
    gain = scale_gain.astype(jnp.float32)

    def normalized(rows):
        rows = rows.astype(jnp.float32)
        return (
            rows * lax.rsqrt(jnp.mean(rows * rows, axis=-1, keepdims=True) + 1e-05) * gain
        ).astype(jnp.bfloat16)

    def doubled(held):
        held = held[None]
        for stage in range(levels):
            arrived = lax.ppermute(held, ("chip", "core"), chip_route(n_chip, n_core, stage, levels))
            held = jnp.concatenate([held, arrived])
        return held

    splits = 2 if capacity % 2 == 0 else 1
    chip_rows = [doubled(normalized(lax.dynamic_index_in_dim(raw, ex_me, 0, keepdims=False)))]
    for k in range(1, n_ex):
        outgoing = lax.dynamic_index_in_dim(raw, (ex_me + k) % n_ex, 0, keepdims=False)
        step = capacity // splits
        halves = []
        for h in range(splits):
            landed = shifted(outgoing[h * step:(h + 1) * step], "ex", n_ex, k)
            halves.append(doubled(normalized(landed)))
        chip_rows.append(jnp.concatenate(halves, axis=1))
    core_rows = [chip_rows] + [
        [shifted(rows, "core", n_core, q) for rows in chip_rows] for q in range(1, n_core)
    ]
    gathered = jnp.stack([jnp.stack(core_rows[q], axis=1) for q in range(n_core)])
    early_in, gathered = lax.optimization_barrier((early_in, gathered))
    flat_rows = gathered.reshape(-1, width)

    gate_part = jnp.dot(flat_rows, gate_cols, preferred_element_type=jnp.float32)
    up_part = jnp.dot(flat_rows, up_cols, preferred_element_type=jnp.float32)
    activated = (jax.nn.silu(gate_part) * up_part).astype(jnp.bfloat16)

    pieces = PIECES if width % (PIECES * 128) == 0 else 1
    span = width // pieces
    got = [[] for _ in range(n_ex)]
    for piece in range(pieces):
        cols = down_rows[:, piece * span:(piece + 1) * span]
        partial_out = jnp.dot(activated, cols, preferred_element_type=jnp.float32).astype(
            jnp.bfloat16
        )
        if piece == 0:
            late_in, selector_in, partial_out = lax.optimization_barrier(
                (late_in, selector_in, partial_out)
            )
        partials = partial_out.reshape(gathered.shape[:-1] + (span,))

        summed = partials[0].astype(jnp.float32)
        for q in range(1, n_core):
            summed = summed + shifted(partials[q], "core", n_core, -q).astype(jnp.float32)
        for stage in reversed(range(levels)):
            half = summed.shape[0] // 2
            sent = summed[half:].astype(SUM_DTYPE)
            arrived = lax.ppermute(sent, ("chip", "core"), chip_route(n_chip, n_core, stage, levels))
            summed = summed[:half] + arrived.astype(jnp.float32)
        reduced = summed[0]

        for k in range(n_ex):
            outgoing = reduced[k].astype(SUM_DTYPE)
            if k == 0:
                got[k].append(shifted(outgoing, "section", sections, 1))
            else:
                route = []
                for s in range(sections):
                    for e in range(n_ex):
                        route.append((s * n_ex + e, ((s + 1) % sections) * n_ex + (e - k) % n_ex))
                got[k].append(lax.ppermute(outgoing, ("section", "ex"), route))
    expert_out = jnp.stack([jnp.concatenate(pieces_k, axis=-1) for pieces_k in got])
    states_in = jnp.concatenate([early_in, late_in])

    branch = jnp.einsum(
        "ect,ecd->td", selector_in, expert_out.astype(jnp.float32), precision=lax.Precision.HIGHEST
    )
    layer_out = (states_in.astype(jnp.float32) + branch).astype(jnp.bfloat16)
    return layer_out[None]


def solution(mesh):
    def run(*args):
        experts = args[5].shape[2]
        sections, ranks = mesh.devices.shape
        owners = ranks // experts
        cores = 2 if owners % 2 == 0 else 1
        devices = mesh.devices.reshape(sections, experts, owners // cores, cores)
        fine = Mesh(devices, ("section", "ex", "chip", "core"))
        dp = ("ex", "chip", "core")
        placed = (
            P("section", dp, None),
            P("section", None),
            P("section", None, dp),
            P("section", None, dp),
            P("section", dp, None),
            P("section", dp, None, None),
            P("section", dp, None),
            P("section", dp, None, None),
        )
        return jax.shard_map(
            body, mesh=fine, in_specs=placed, out_specs=P("section", dp, None), check_vma=False
        )(*args)

    return run
```

```python
import jax
import jax.numpy as jnp
from jax import lax
from jax.sharding import Mesh, PartitionSpec as P

SUM_DTYPE = jnp.bfloat16
PIECES = 1


def shifted(block, axes, size, distance):
    route = [(i, (i + distance) % size) for i in range(size)]
    return lax.ppermute(block, axes, route)


def chip_route(n_chip, n_core, stage, levels):
    route = []
    for k in range(n_chip):
        for c in range(n_core):
            bit = (stage + c) % levels
            route.append((k * n_core + c, (k ^ (1 << bit)) * n_core + c))
    return route


def body(
    hidden_states,
    norm_gain,
    gate_weight,
    up_weight,
    down_weight,
    route_rows,
    route_count,
    route_gate,
):
    states = hidden_states[0]
    scale_gain = norm_gain[0]
    gate_cols = gate_weight[0]
    up_cols = up_weight[0]
    down_rows = down_weight[0]
    slot_rows = route_rows[0, 0]
    live_count = route_count[0, 0]
    slot_gates = route_gate[0, 0]
    tok_count, width = states.shape
    experts, capacity = slot_rows.shape
    sections = lax.axis_size("section")
    n_ex = lax.axis_size("ex")
    n_chip = lax.axis_size("chip")
    n_core = lax.axis_size("core")
    levels = n_chip.bit_length() - 1
    ex_me = lax.axis_index("ex")

    live_mask = jnp.arange(capacity)[None, :] < live_count[:, None]
    weighting = jnp.where(live_mask, slot_gates, 0.0)
    selector_out = (slot_rows[..., None] == jnp.arange(tok_count)[None, None, :]).astype(
        jnp.float32
    ) * weighting[..., None]
    order = (ex_me + jnp.arange(n_ex)) % n_ex
    selector_out = jnp.take(selector_out, order, axis=0)
    early_in = shifted(states[: tok_count // 2], "section", sections, 1)
    late_in = shifted(states[tok_count // 2 :], "section", sections, 1)
    selector_in = shifted(selector_out, "section", sections, 1)

    selector = (slot_rows.reshape(-1)[:, None] == jnp.arange(tok_count)[None, :]).astype(states.dtype)
    raw = jnp.dot(selector, states, preferred_element_type=jnp.float32).astype(states.dtype)
    raw = raw.reshape(experts, capacity, width)
    gain = scale_gain.astype(jnp.float32)

    def normalized(rows):
        rows = rows.astype(jnp.float32)
        return (
            rows * lax.rsqrt(jnp.mean(rows * rows, axis=-1, keepdims=True) + 1e-05) * gain
        ).astype(jnp.bfloat16)

    def doubled(held):
        held = held[None]
        for stage in range(levels):
            arrived = lax.ppermute(held, ("chip", "core"), chip_route(n_chip, n_core, stage, levels))
            held = jnp.concatenate([held, arrived])
        return held

    splits = 2 if capacity % 2 == 0 else 1
    chip_rows = [doubled(normalized(lax.dynamic_index_in_dim(raw, ex_me, 0, keepdims=False)))]
    for k in range(1, n_ex):
        outgoing = lax.dynamic_index_in_dim(raw, (ex_me + k) % n_ex, 0, keepdims=False)
        step = capacity // splits
        halves = []
        for h in range(splits):
            landed = shifted(outgoing[h * step:(h + 1) * step], "ex", n_ex, k)
            halves.append(doubled(normalized(landed)))
        chip_rows.append(jnp.concatenate(halves, axis=1))
    core_rows = [chip_rows] + [
        [shifted(rows, "core", n_core, q) for rows in chip_rows] for q in range(1, n_core)
    ]
    gathered = jnp.stack([jnp.stack(core_rows[q], axis=1) for q in range(n_core)])
    early_in, gathered = lax.optimization_barrier((early_in, gathered))
    flat_rows = gathered.reshape(-1, width)

    gate_part = jnp.dot(flat_rows, gate_cols, preferred_element_type=jnp.float32)
    up_part = jnp.dot(flat_rows, up_cols, preferred_element_type=jnp.float32)
    activated = (jax.nn.silu(gate_part) * up_part).astype(jnp.bfloat16)

    pieces = PIECES if width % (PIECES * 128) == 0 else 1
    span = width // pieces
    got = [[] for _ in range(n_ex)]
    for piece in range(pieces):
        cols = down_rows[:, piece * span:(piece + 1) * span]
        partial_out = jnp.dot(activated, cols, preferred_element_type=jnp.float32).astype(
            jnp.bfloat16
        )
        if piece == 0:
            late_in, selector_in, partial_out = lax.optimization_barrier(
                (late_in, selector_in, partial_out)
            )
        partials = partial_out.reshape(gathered.shape[:-1] + (span,))

        summed = partials[0].astype(jnp.float32)
        for q in range(1, n_core):
            summed = summed + shifted(partials[q], "core", n_core, -q).astype(jnp.float32)
        for stage in reversed(range(levels)):
            half = summed.shape[0] // 2
            sent = summed[half:].astype(SUM_DTYPE)
            arrived = lax.ppermute(sent, ("chip", "core"), chip_route(n_chip, n_core, stage, levels))
            summed = summed[:half] + arrived.astype(jnp.float32)
        reduced = summed[0]

        for k in range(n_ex):
            outgoing = reduced[k].astype(SUM_DTYPE)
            if k == 0:
                got[k].append(shifted(outgoing, "section", sections, 1))
            else:
                route = []
                for s in range(sections):
                    for e in range(n_ex):
                        route.append((s * n_ex + e, ((s + 1) % sections) * n_ex + (e - k) % n_ex))
                got[k].append(lax.ppermute(outgoing, ("section", "ex"), route))
    expert_out = jnp.stack([jnp.concatenate(pieces_k, axis=-1) for pieces_k in got])
    states_in = jnp.concatenate([early_in, late_in])

    branch = jnp.einsum(
        "ect,ecd->td", selector_in, expert_out.astype(jnp.float32), precision=lax.Precision.HIGHEST
    )
    layer_out = (states_in.astype(jnp.float32) + branch).astype(jnp.bfloat16)
    return layer_out[None]


def solution(mesh):
    def run(*args):
        experts = args[5].shape[2]
        sections, ranks = mesh.devices.shape
        owners = ranks // experts
        cores = 2 if owners % 2 == 0 else 1
        devices = mesh.devices.reshape(sections, experts, owners // cores, cores)
        fine = Mesh(devices, ("section", "ex", "chip", "core"))
        dp = ("ex", "chip", "core")
        placed = (
            P("section", dp, None),
            P("section", None),
            P("section", None, dp),
            P("section", None, dp),
            P("section", dp, None),
            P("section", dp, None, None),
            P("section", dp, None),
            P("section", dp, None, None),
        )
        return jax.shard_map(
            body, mesh=fine, in_specs=placed, out_specs=P("section", dp, None), check_vma=False
        )(*args)

    return run
```

```python
import jax
import jax.numpy as jnp
from jax import lax
from jax.sharding import Mesh, PartitionSpec as P

SUM_DTYPE = jnp.bfloat16
PIECES = 2


def shifted(block, axes, size, distance):
    route = [(i, (i + distance) % size) for i in range(size)]
    return lax.ppermute(block, axes, route)


def chip_route(n_chip, n_core, stage, levels):
    route = []
    for k in range(n_chip):
        for c in range(n_core):
            bit = (stage + c) % levels
            route.append((k * n_core + c, (k ^ (1 << bit)) * n_core + c))
    return route


def body(
    hidden_states,
    norm_gain,
    gate_weight,
    up_weight,
    down_weight,
    route_rows,
    route_count,
    route_gate,
):
    states = hidden_states[0]
    scale_gain = norm_gain[0]
    gate_cols = gate_weight[0]
    up_cols = up_weight[0]
    down_rows = down_weight[0]
    slot_rows = route_rows[0, 0]
    live_count = route_count[0, 0]
    slot_gates = route_gate[0, 0]
    tok_count, width = states.shape
    experts, capacity = slot_rows.shape
    sections = lax.axis_size("section")
    n_ex = lax.axis_size("ex")
    n_chip = lax.axis_size("chip")
    n_core = lax.axis_size("core")
    levels = n_chip.bit_length() - 1
    ex_me = lax.axis_index("ex")

    live_mask = jnp.arange(capacity)[None, :] < live_count[:, None]
    weighting = jnp.where(live_mask, slot_gates, 0.0)
    selector_out = (slot_rows[..., None] == jnp.arange(tok_count)[None, None, :]).astype(
        jnp.float32
    ) * weighting[..., None]
    order = (ex_me + jnp.arange(n_ex)) % n_ex
    selector_out = jnp.take(selector_out, order, axis=0)
    early_in = shifted(states[: tok_count // 2], "section", sections, 1)
    late_in = shifted(states[tok_count // 2 :], "section", sections, 1)
    selector_in = shifted(selector_out, "section", sections, 1)

    selector = (slot_rows.reshape(-1)[:, None] == jnp.arange(tok_count)[None, :]).astype(states.dtype)
    raw = jnp.dot(selector, states, preferred_element_type=jnp.float32).astype(states.dtype)
    raw = raw.reshape(experts, capacity, width)
    gain = scale_gain.astype(jnp.float32)

    def normalized(rows):
        rows = rows.astype(jnp.float32)
        return (
            rows * lax.rsqrt(jnp.mean(rows * rows, axis=-1, keepdims=True) + 1e-05) * gain
        ).astype(jnp.bfloat16)

    def doubled(held):
        held = held[None]
        for stage in range(levels):
            arrived = lax.ppermute(held, ("chip", "core"), chip_route(n_chip, n_core, stage, levels))
            held = jnp.concatenate([held, arrived])
        return held

    splits = 2 if capacity % 2 == 0 else 1
    own_rows = doubled(normalized(lax.dynamic_index_in_dim(raw, ex_me, 0, keepdims=False)))
    step = capacity // splits
    landed = []
    for k in range(1, n_ex):
        outgoing = lax.dynamic_index_in_dim(raw, (ex_me + k) % n_ex, 0, keepdims=False)
        landed.append(
            [shifted(outgoing[h * step:(h + 1) * step], "ex", n_ex, k) for h in range(splits)]
        )
    own_rows, landed = lax.optimization_barrier((own_rows, landed))
    chip_rows = [own_rows]
    for halves in landed:
        chip_rows.append(jnp.concatenate([doubled(normalized(h)) for h in halves], axis=1))
    core_rows = [chip_rows] + [
        [shifted(rows, "core", n_core, q) for rows in chip_rows] for q in range(1, n_core)
    ]
    gathered = jnp.stack([jnp.stack(core_rows[q], axis=1) for q in range(n_core)])
    early_in, gathered = lax.optimization_barrier((early_in, gathered))
    flat_rows = gathered.reshape(-1, width)

    gate_part = jnp.dot(flat_rows, gate_cols, preferred_element_type=jnp.float32)
    up_part = jnp.dot(flat_rows, up_cols, preferred_element_type=jnp.float32)
    activated = (jax.nn.silu(gate_part) * up_part).astype(jnp.bfloat16)

    pieces = PIECES if width % (PIECES * 128) == 0 else 1
    span = width // pieces
    got = [[] for _ in range(n_ex)]
    for piece in range(pieces):
        cols = down_rows[:, piece * span:(piece + 1) * span]
        partial_out = jnp.dot(activated, cols, preferred_element_type=jnp.float32).astype(
            jnp.bfloat16
        )
        if piece == 0:
            late_in, selector_in, partial_out = lax.optimization_barrier(
                (late_in, selector_in, partial_out)
            )
        partials = partial_out.reshape(gathered.shape[:-1] + (span,))

        summed = partials[0].astype(jnp.float32)
        for q in range(1, n_core):
            summed = summed + shifted(partials[q], "core", n_core, -q).astype(jnp.float32)
        for stage in reversed(range(levels)):
            half = summed.shape[0] // 2
            sent = summed[half:].astype(SUM_DTYPE)
            arrived = lax.ppermute(sent, ("chip", "core"), chip_route(n_chip, n_core, stage, levels))
            summed = summed[:half] + arrived.astype(jnp.float32)
        reduced = summed[0]

        for k in range(n_ex):
            outgoing = reduced[k].astype(SUM_DTYPE)
            if k == 0:
                got[k].append(shifted(outgoing, "section", sections, 1))
            else:
                route = []
                for s in range(sections):
                    for e in range(n_ex):
                        route.append((s * n_ex + e, ((s + 1) % sections) * n_ex + (e - k) % n_ex))
                got[k].append(lax.ppermute(outgoing, ("section", "ex"), route))
    expert_out = jnp.stack([jnp.concatenate(pieces_k, axis=-1) for pieces_k in got])
    states_in = jnp.concatenate([early_in, late_in])

    branch = jnp.einsum(
        "ect,ecd->td", selector_in, expert_out.astype(jnp.float32), precision=lax.Precision.HIGHEST
    )
    layer_out = (states_in.astype(jnp.float32) + branch).astype(jnp.bfloat16)
    return layer_out[None]


def solution(mesh):
    def run(*args):
        experts = args[5].shape[2]
        sections, ranks = mesh.devices.shape
        owners = ranks // experts
        cores = 2 if owners % 2 == 0 else 1
        devices = mesh.devices.reshape(sections, experts, owners // cores, cores)
        fine = Mesh(devices, ("section", "ex", "chip", "core"))
        dp = ("ex", "chip", "core")
        placed = (
            P("section", dp, None),
            P("section", None),
            P("section", None, dp),
            P("section", None, dp),
            P("section", dp, None),
            P("section", dp, None, None),
            P("section", dp, None),
            P("section", dp, None, None),
        )
        return jax.shard_map(
            body, mesh=fine, in_specs=placed, out_specs=P("section", dp, None), check_vma=False
        )(*args)

    return run
```

```python
import jax
import jax.numpy as jnp
from jax import lax
from jax.sharding import Mesh, PartitionSpec as P

SUM_DTYPE = jnp.bfloat16
PIECES = 2


def shifted(block, axes, size, distance):
    route = [(i, (i + distance) % size) for i in range(size)]
    return lax.ppermute(block, axes, route)


def chip_route(n_chip, n_core, stage, levels):
    route = []
    for k in range(n_chip):
        for c in range(n_core):
            bit = (stage + c) % levels
            route.append((k * n_core + c, (k ^ (1 << bit)) * n_core + c))
    return route


def body(
    hidden_states,
    norm_gain,
    gate_weight,
    up_weight,
    down_weight,
    route_rows,
    route_count,
    route_gate,
):
    states = hidden_states[0]
    scale_gain = norm_gain[0]
    gate_cols = gate_weight[0]
    up_cols = up_weight[0]
    down_rows = down_weight[0]
    slot_rows = route_rows[0, 0]
    live_count = route_count[0, 0]
    slot_gates = route_gate[0, 0]
    tok_count, width = states.shape
    experts, capacity = slot_rows.shape
    sections = lax.axis_size("section")
    n_ex = lax.axis_size("ex")
    n_chip = lax.axis_size("chip")
    n_core = lax.axis_size("core")
    levels = n_chip.bit_length() - 1
    ex_me = lax.axis_index("ex")

    live_mask = jnp.arange(capacity)[None, :] < live_count[:, None]
    weighting = jnp.where(live_mask, slot_gates, 0.0)
    selector_out = (slot_rows[..., None] == jnp.arange(tok_count)[None, None, :]).astype(
        jnp.float32
    ) * weighting[..., None]
    order = (ex_me + jnp.arange(n_ex)) % n_ex
    selector_out = jnp.take(selector_out, order, axis=0)
    early_in = shifted(states[: tok_count // 2], "section", sections, 1)
    late_in = shifted(states[tok_count // 2 :], "section", sections, 1)
    selector_in = shifted(selector_out, "section", sections, 1)

    selector = (slot_rows.reshape(-1)[:, None] == jnp.arange(tok_count)[None, :]).astype(states.dtype)
    raw = jnp.dot(selector, states, preferred_element_type=jnp.float32).astype(states.dtype)
    raw = raw.reshape(experts, capacity, width)
    gain = scale_gain.astype(jnp.float32)

    def normalized(rows):
        rows = rows.astype(jnp.float32)
        return (
            rows * lax.rsqrt(jnp.mean(rows * rows, axis=-1, keepdims=True) + 1e-05) * gain
        ).astype(jnp.bfloat16)

    def doubled(held):
        held = held[None]
        for stage in range(levels):
            arrived = lax.ppermute(held, ("chip", "core"), chip_route(n_chip, n_core, stage, levels))
            held = jnp.concatenate([held, arrived])
        return held

    splits = 2 if capacity % 2 == 0 else 1
    chip_rows = [doubled(normalized(lax.dynamic_index_in_dim(raw, ex_me, 0, keepdims=False)))]
    for k in range(1, n_ex):
        outgoing = lax.dynamic_index_in_dim(raw, (ex_me + k) % n_ex, 0, keepdims=False)
        step = capacity // splits
        halves = []
        for h in range(splits):
            landed = shifted(outgoing[h * step:(h + 1) * step], "ex", n_ex, k)
            halves.append(doubled(normalized(landed)))
        chip_rows.append(jnp.concatenate(halves, axis=1))
    core_rows = [chip_rows] + [
        [shifted(rows, "core", n_core, q) for rows in chip_rows] for q in range(1, n_core)
    ]
    gathered = jnp.stack([jnp.stack(core_rows[q], axis=1) for q in range(n_core)])
    early_in, gathered = lax.optimization_barrier((early_in, gathered))
    flat_rows = gathered.reshape(-1, width)

    gate_part = jnp.dot(flat_rows, gate_cols, preferred_element_type=jnp.float32)
    up_part = jnp.dot(flat_rows, up_cols, preferred_element_type=jnp.float32)
    activated = (jax.nn.silu(gate_part) * up_part).astype(jnp.bfloat16)

    pieces = PIECES if width % (PIECES * 128) == 0 else 1
    span = width // pieces
    got = [[] for _ in range(n_ex)]
    for piece in range(pieces):
        cols = down_rows[:, piece * span:(piece + 1) * span]
        partial_out = jnp.dot(activated, cols, preferred_element_type=jnp.float32).astype(
            jnp.bfloat16
        )
        if piece == 0:
            late_in, selector_in, partial_out = lax.optimization_barrier(
                (late_in, selector_in, partial_out)
            )
        partials = partial_out.reshape(gathered.shape[:-1] + (span,))

        summed = partials[0].astype(jnp.float32)
        for q in range(1, n_core):
            summed = summed + shifted(partials[q], "core", n_core, -q).astype(jnp.float32)
        if piece + 1 < pieces:
            summed, activated = lax.optimization_barrier((summed, activated))
        for stage in reversed(range(levels)):
            half = summed.shape[0] // 2
            sent = summed[half:].astype(SUM_DTYPE)
            arrived = lax.ppermute(sent, ("chip", "core"), chip_route(n_chip, n_core, stage, levels))
            summed = summed[:half] + arrived.astype(jnp.float32)
        reduced = summed[0]

        for k in range(n_ex):
            outgoing = reduced[k].astype(SUM_DTYPE)
            if k == 0:
                got[k].append(shifted(outgoing, "section", sections, 1))
            else:
                route = []
                for s in range(sections):
                    for e in range(n_ex):
                        route.append((s * n_ex + e, ((s + 1) % sections) * n_ex + (e - k) % n_ex))
                got[k].append(lax.ppermute(outgoing, ("section", "ex"), route))
    expert_out = jnp.stack([jnp.concatenate(pieces_k, axis=-1) for pieces_k in got])
    states_in = jnp.concatenate([early_in, late_in])

    branch = jnp.einsum(
        "ect,ecd->td", selector_in, expert_out.astype(jnp.float32), precision=lax.Precision.HIGHEST
    )
    layer_out = (states_in.astype(jnp.float32) + branch).astype(jnp.bfloat16)
    return layer_out[None]


def solution(mesh):
    def run(*args):
        experts = args[5].shape[2]
        sections, ranks = mesh.devices.shape
        owners = ranks // experts
        cores = 2 if owners % 2 == 0 else 1
        devices = mesh.devices.reshape(sections, experts, owners // cores, cores)
        fine = Mesh(devices, ("section", "ex", "chip", "core"))
        dp = ("ex", "chip", "core")
        placed = (
            P("section", dp, None),
            P("section", None),
            P("section", None, dp),
            P("section", None, dp),
            P("section", dp, None),
            P("section", dp, None, None),
            P("section", dp, None),
            P("section", dp, None, None),
        )
        return jax.shard_map(
            body, mesh=fine, in_specs=placed, out_specs=P("section", dp, None), check_vma=False
        )(*args)

    return run
```

```python
import jax
import jax.numpy as jnp
from jax import lax
from jax.sharding import Mesh, PartitionSpec as P

SUM_DTYPE = jnp.bfloat16
PIECES = 3


def shifted(block, axes, size, distance):
    route = [(i, (i + distance) % size) for i in range(size)]
    return lax.ppermute(block, axes, route)


def chip_route(n_chip, n_core, stage, levels):
    route = []
    for k in range(n_chip):
        for c in range(n_core):
            bit = (stage + c) % levels
            route.append((k * n_core + c, (k ^ (1 << bit)) * n_core + c))
    return route


def body(
    hidden_states,
    norm_gain,
    gate_weight,
    up_weight,
    down_weight,
    route_rows,
    route_count,
    route_gate,
):
    states = hidden_states[0]
    scale_gain = norm_gain[0]
    gate_cols = gate_weight[0]
    up_cols = up_weight[0]
    down_rows = down_weight[0]
    slot_rows = route_rows[0, 0]
    live_count = route_count[0, 0]
    slot_gates = route_gate[0, 0]
    tok_count, width = states.shape
    experts, capacity = slot_rows.shape
    sections = lax.axis_size("section")
    n_ex = lax.axis_size("ex")
    n_chip = lax.axis_size("chip")
    n_core = lax.axis_size("core")
    levels = n_chip.bit_length() - 1
    ex_me = lax.axis_index("ex")

    live_mask = jnp.arange(capacity)[None, :] < live_count[:, None]
    weighting = jnp.where(live_mask, slot_gates, 0.0)
    selector_out = (slot_rows[..., None] == jnp.arange(tok_count)[None, None, :]).astype(
        jnp.float32
    ) * weighting[..., None]
    order = (ex_me + jnp.arange(n_ex)) % n_ex
    selector_out = jnp.take(selector_out, order, axis=0)
    early_in = shifted(states[: tok_count // 2], "section", sections, 1)
    late_in = shifted(states[tok_count // 2 :], "section", sections, 1)
    selector_in = shifted(selector_out, "section", sections, 1)

    selector = (slot_rows.reshape(-1)[:, None] == jnp.arange(tok_count)[None, :]).astype(states.dtype)
    raw = jnp.dot(selector, states, preferred_element_type=jnp.float32).astype(states.dtype)
    raw = raw.reshape(experts, capacity, width)
    gain = scale_gain.astype(jnp.float32)

    def normalized(rows):
        rows = rows.astype(jnp.float32)
        return (
            rows * lax.rsqrt(jnp.mean(rows * rows, axis=-1, keepdims=True) + 1e-05) * gain
        ).astype(jnp.bfloat16)

    def doubled(held):
        held = held[None]
        for stage in range(levels):
            arrived = lax.ppermute(held, ("chip", "core"), chip_route(n_chip, n_core, stage, levels))
            held = jnp.concatenate([held, arrived])
        return held

    splits = 2 if capacity % 2 == 0 else 1
    chip_rows = [doubled(normalized(lax.dynamic_index_in_dim(raw, ex_me, 0, keepdims=False)))]
    for k in range(1, n_ex):
        outgoing = lax.dynamic_index_in_dim(raw, (ex_me + k) % n_ex, 0, keepdims=False)
        step = capacity // splits
        halves = []
        for h in range(splits):
            landed = shifted(outgoing[h * step:(h + 1) * step], "ex", n_ex, k)
            halves.append(doubled(normalized(landed)))
        chip_rows.append(jnp.concatenate(halves, axis=1))
    core_rows = [chip_rows] + [
        [shifted(rows, "core", n_core, q) for rows in chip_rows] for q in range(1, n_core)
    ]
    gathered = jnp.stack([jnp.stack(core_rows[q], axis=1) for q in range(n_core)])
    early_in, gathered = lax.optimization_barrier((early_in, gathered))
    flat_rows = gathered.reshape(-1, width)

    gate_part = jnp.dot(flat_rows, gate_cols, preferred_element_type=jnp.float32)
    up_part = jnp.dot(flat_rows, up_cols, preferred_element_type=jnp.float32)
    activated = (jax.nn.silu(gate_part) * up_part).astype(jnp.bfloat16)

    pieces = PIECES if width % (PIECES * 128) == 0 else 1
    span = width // pieces
    got = [[] for _ in range(n_ex)]
    for piece in range(pieces):
        cols = down_rows[:, piece * span:(piece + 1) * span]
        partial_out = jnp.dot(activated, cols, preferred_element_type=jnp.float32).astype(
            jnp.bfloat16
        )
        if piece == 0:
            late_in, selector_in, partial_out = lax.optimization_barrier(
                (late_in, selector_in, partial_out)
            )
        partials = partial_out.reshape(gathered.shape[:-1] + (span,))

        summed = partials[0].astype(jnp.float32)
        for q in range(1, n_core):
            summed = summed + shifted(partials[q], "core", n_core, -q).astype(jnp.float32)
        for stage in reversed(range(levels)):
            half = summed.shape[0] // 2
            sent = summed[half:].astype(SUM_DTYPE)
            arrived = lax.ppermute(sent, ("chip", "core"), chip_route(n_chip, n_core, stage, levels))
            summed = summed[:half] + arrived.astype(jnp.float32)
        reduced = summed[0]

        for k in range(n_ex):
            outgoing = reduced[k].astype(SUM_DTYPE)
            if k == 0:
                got[k].append(shifted(outgoing, "section", sections, 1))
            else:
                route = []
                for s in range(sections):
                    for e in range(n_ex):
                        route.append((s * n_ex + e, ((s + 1) % sections) * n_ex + (e - k) % n_ex))
                got[k].append(lax.ppermute(outgoing, ("section", "ex"), route))
    expert_out = jnp.stack([jnp.concatenate(pieces_k, axis=-1) for pieces_k in got])
    states_in = jnp.concatenate([early_in, late_in])

    branch = jnp.einsum(
        "ect,ecd->td", selector_in, expert_out.astype(jnp.float32), precision=lax.Precision.HIGHEST
    )
    layer_out = (states_in.astype(jnp.float32) + branch).astype(jnp.bfloat16)
    return layer_out[None]


def solution(mesh):
    def run(*args):
        experts = args[5].shape[2]
        sections, ranks = mesh.devices.shape
        owners = ranks // experts
        cores = 2 if owners % 2 == 0 else 1
        devices = mesh.devices.reshape(sections, experts, owners // cores, cores)
        fine = Mesh(devices, ("section", "ex", "chip", "core"))
        dp = ("ex", "chip", "core")
        placed = (
            P("section", dp, None),
            P("section", None),
            P("section", None, dp),
            P("section", None, dp),
            P("section", dp, None),
            P("section", dp, None, None),
            P("section", dp, None),
            P("section", dp, None, None),
        )
        return jax.shard_map(
            body, mesh=fine, in_specs=placed, out_specs=P("section", dp, None), check_vma=False
        )(*args)

    return run
```

```python
import jax
import jax.numpy as jnp
from jax import lax
from jax.sharding import Mesh, PartitionSpec as P

SUM_DTYPE = jnp.bfloat16
PIECES = 2


def shifted(block, axes, size, distance):
    route = [(i, (i + distance) % size) for i in range(size)]
    return lax.ppermute(block, axes, route)


def chip_route(n_chip, n_core, stage, levels):
    route = []
    for k in range(n_chip):
        for c in range(n_core):
            bit = (stage + c) % levels
            route.append((k * n_core + c, (k ^ (1 << bit)) * n_core + c))
    return route


def body(
    hidden_states,
    norm_gain,
    gate_weight,
    up_weight,
    down_weight,
    route_rows,
    route_count,
    route_gate,
):
    states = hidden_states[0]
    scale_gain = norm_gain[0]
    gate_cols = gate_weight[0]
    up_cols = up_weight[0]
    down_rows = down_weight[0]
    slot_rows = route_rows[0, 0]
    live_count = route_count[0, 0]
    slot_gates = route_gate[0, 0]
    tok_count, width = states.shape
    experts, capacity = slot_rows.shape
    sections = lax.axis_size("section")
    n_ex = lax.axis_size("ex")
    n_chip = lax.axis_size("chip")
    n_core = lax.axis_size("core")
    levels = n_chip.bit_length() - 1
    ex_me = lax.axis_index("ex")

    live_mask = jnp.arange(capacity)[None, :] < live_count[:, None]
    weighting = jnp.where(live_mask, slot_gates, 0.0)
    selector_out = (slot_rows[..., None] == jnp.arange(tok_count)[None, None, :]).astype(
        jnp.float32
    ) * weighting[..., None]
    order = (ex_me + jnp.arange(n_ex)) % n_ex
    selector_out = jnp.take(selector_out, order, axis=0)
    early_in = shifted(states[: tok_count // 2], "section", sections, 1)
    late_in = shifted(states[tok_count // 2 :], "section", sections, 1)
    selector_in = shifted(selector_out, "section", sections, 1)

    selector = (slot_rows.reshape(-1)[:, None] == jnp.arange(tok_count)[None, :]).astype(states.dtype)
    raw = jnp.dot(selector, states, preferred_element_type=jnp.float32).astype(states.dtype)
    raw = raw.reshape(experts, capacity, width)
    gain = scale_gain.astype(jnp.float32)

    def normalized(rows):
        rows = rows.astype(jnp.float32)
        return (
            rows * lax.rsqrt(jnp.mean(rows * rows, axis=-1, keepdims=True) + 1e-05) * gain
        ).astype(jnp.bfloat16)

    def doubled(held):
        held = held[None]
        for stage in range(levels):
            arrived = lax.ppermute(held, ("chip", "core"), chip_route(n_chip, n_core, stage, levels))
            held = jnp.concatenate([held, arrived])
        return held

    splits = 1
    chip_rows = [doubled(normalized(lax.dynamic_index_in_dim(raw, ex_me, 0, keepdims=False)))]
    for k in range(1, n_ex):
        outgoing = lax.dynamic_index_in_dim(raw, (ex_me + k) % n_ex, 0, keepdims=False)
        step = capacity // splits
        halves = []
        for h in range(splits):
            landed = shifted(outgoing[h * step:(h + 1) * step], "ex", n_ex, k)
            halves.append(doubled(normalized(landed)))
        chip_rows.append(jnp.concatenate(halves, axis=1))
    core_rows = [chip_rows] + [
        [shifted(rows, "core", n_core, q) for rows in chip_rows] for q in range(1, n_core)
    ]
    gathered = jnp.stack([jnp.stack(core_rows[q], axis=1) for q in range(n_core)])
    early_in, gathered = lax.optimization_barrier((early_in, gathered))
    flat_rows = gathered.reshape(-1, width)

    gate_part = jnp.dot(flat_rows, gate_cols, preferred_element_type=jnp.float32)
    up_part = jnp.dot(flat_rows, up_cols, preferred_element_type=jnp.float32)
    activated = (jax.nn.silu(gate_part) * up_part).astype(jnp.bfloat16)

    pieces = PIECES if width % (PIECES * 128) == 0 else 1
    span = width // pieces
    got = [[] for _ in range(n_ex)]
    for piece in range(pieces):
        cols = down_rows[:, piece * span:(piece + 1) * span]
        partial_out = jnp.dot(activated, cols, preferred_element_type=jnp.float32).astype(
            jnp.bfloat16
        )
        if piece == 0:
            late_in, selector_in, partial_out = lax.optimization_barrier(
                (late_in, selector_in, partial_out)
            )
        partials = partial_out.reshape(gathered.shape[:-1] + (span,))

        summed = partials[0].astype(jnp.float32)
        for q in range(1, n_core):
            summed = summed + shifted(partials[q], "core", n_core, -q).astype(jnp.float32)
        for stage in reversed(range(levels)):
            half = summed.shape[0] // 2
            sent = summed[half:].astype(SUM_DTYPE)
            arrived = lax.ppermute(sent, ("chip", "core"), chip_route(n_chip, n_core, stage, levels))
            summed = summed[:half] + arrived.astype(jnp.float32)
        reduced = summed[0]

        for k in range(n_ex):
            outgoing = reduced[k].astype(SUM_DTYPE)
            if k == 0:
                got[k].append(shifted(outgoing, "section", sections, 1))
            else:
                route = []
                for s in range(sections):
                    for e in range(n_ex):
                        route.append((s * n_ex + e, ((s + 1) % sections) * n_ex + (e - k) % n_ex))
                got[k].append(lax.ppermute(outgoing, ("section", "ex"), route))
    expert_out = jnp.stack([jnp.concatenate(pieces_k, axis=-1) for pieces_k in got])
    states_in = jnp.concatenate([early_in, late_in])

    branch = jnp.einsum(
        "ect,ecd->td", selector_in, expert_out.astype(jnp.float32), precision=lax.Precision.HIGHEST
    )
    layer_out = (states_in.astype(jnp.float32) + branch).astype(jnp.bfloat16)
    return layer_out[None]


def solution(mesh):
    def run(*args):
        experts = args[5].shape[2]
        sections, ranks = mesh.devices.shape
        owners = ranks // experts
        cores = 2 if owners % 2 == 0 else 1
        devices = mesh.devices.reshape(sections, experts, owners // cores, cores)
        fine = Mesh(devices, ("section", "ex", "chip", "core"))
        dp = ("ex", "chip", "core")
        placed = (
            P("section", dp, None),
            P("section", None),
            P("section", None, dp),
            P("section", None, dp),
            P("section", dp, None),
            P("section", dp, None, None),
            P("section", dp, None),
            P("section", dp, None, None),
        )
        return jax.shard_map(
            body, mesh=fine, in_specs=placed, out_specs=P("section", dp, None), check_vma=False
        )(*args)

    return run
```

```python
import jax
import jax.numpy as jnp
from jax import lax
from jax.sharding import Mesh, PartitionSpec as P

SUM_DTYPE = jnp.bfloat16
PIECES = 2


def shifted(block, axes, size, distance):
    route = [(i, (i + distance) % size) for i in range(size)]
    return lax.ppermute(block, axes, route)


def chip_route(n_chip, n_core, stage, levels):
    route = []
    for k in range(n_chip):
        for c in range(n_core):
            bit = (stage + c) % levels
            route.append((k * n_core + c, (k ^ (1 << bit)) * n_core + c))
    return route


def body(
    hidden_states,
    norm_gain,
    gate_weight,
    up_weight,
    down_weight,
    route_rows,
    route_count,
    route_gate,
):
    states = hidden_states[0]
    scale_gain = norm_gain[0]
    gate_cols = gate_weight[0]
    up_cols = up_weight[0]
    down_rows = down_weight[0]
    slot_rows = route_rows[0, 0]
    live_count = route_count[0, 0]
    slot_gates = route_gate[0, 0]
    tok_count, width = states.shape
    experts, capacity = slot_rows.shape
    sections = lax.axis_size("section")
    n_ex = lax.axis_size("ex")
    n_chip = lax.axis_size("chip")
    n_core = lax.axis_size("core")
    levels = n_chip.bit_length() - 1
    ex_me = lax.axis_index("ex")

    live_mask = jnp.arange(capacity)[None, :] < live_count[:, None]
    weighting = jnp.where(live_mask, slot_gates, 0.0)
    selector_out = (slot_rows[..., None] == jnp.arange(tok_count)[None, None, :]).astype(
        jnp.float32
    ) * weighting[..., None]
    order = (ex_me + jnp.arange(n_ex)) % n_ex
    selector_out = jnp.take(selector_out, order, axis=0)
    early_in = shifted(states[: tok_count // 2], "section", sections, 1)
    late_in = shifted(states[tok_count // 2 :], "section", sections, 1)
    selector_in = shifted(selector_out, "section", sections, 1)

    selector = (slot_rows.reshape(-1)[:, None] == jnp.arange(tok_count)[None, :]).astype(states.dtype)
    raw = jnp.dot(selector, states, preferred_element_type=jnp.float32).astype(states.dtype)
    raw = raw.reshape(experts, capacity, width)
    gain = scale_gain.astype(jnp.float32)

    def normalized(rows):
        rows = rows.astype(jnp.float32)
        return (
            rows * lax.rsqrt(jnp.mean(rows * rows, axis=-1, keepdims=True) + 1e-05) * gain
        ).astype(jnp.bfloat16)

    def doubled(held):
        held = held[None]
        for stage in range(levels):
            arrived = lax.ppermute(held, ("chip", "core"), chip_route(n_chip, n_core, stage, levels))
            held = jnp.concatenate([held, arrived])
        return held

    splits = 2 if capacity % 2 == 0 else 1
    chip_rows = [doubled(normalized(lax.dynamic_index_in_dim(raw, ex_me, 0, keepdims=False)))]
    for k in range(1, n_ex):
        outgoing = lax.dynamic_index_in_dim(raw, (ex_me + k) % n_ex, 0, keepdims=False)
        step = capacity // splits
        halves = []
        for h in range(splits):
            landed = shifted(outgoing[h * step:(h + 1) * step], "ex", n_ex, k)
            halves.append(doubled(normalized(landed)))
        chip_rows.append(jnp.concatenate(halves, axis=1))
    core_rows = [chip_rows] + [
        [shifted(rows, "core", n_core, q) for rows in chip_rows] for q in range(1, n_core)
    ]
    gathered = jnp.stack([jnp.stack(core_rows[q], axis=1) for q in range(n_core)])
    early_in, gathered = lax.optimization_barrier((early_in, gathered))
    flat_rows = gathered.reshape(-1, width)

    gate_part = jnp.dot(flat_rows, gate_cols, preferred_element_type=jnp.float32)
    up_part = jnp.dot(flat_rows, up_cols, preferred_element_type=jnp.float32)
    activated = (jax.nn.silu(gate_part) * up_part).astype(jnp.bfloat16)

    pieces = PIECES if width % (PIECES * 128) == 0 else 1
    span = width // pieces
    got = [[] for _ in range(n_ex)]
    for piece in range(pieces):
        cols = down_rows[:, piece * span:(piece + 1) * span]
        partial_out = jnp.dot(activated, cols, preferred_element_type=jnp.float32).astype(
            jnp.bfloat16
        )
        if piece == 0:
            late_in, selector_in, partial_out = lax.optimization_barrier(
                (late_in, selector_in, partial_out)
            )
        partials = partial_out.reshape(gathered.shape[:-1] + (span,))

        summed = partials[0].astype(jnp.float32)
        for q in range(1, n_core):
            summed = summed + shifted(partials[q], "core", n_core, -q).astype(jnp.float32)
        for stage in reversed(range(levels)):
            half = summed.shape[0] // 2
            sent = summed[half:].astype(SUM_DTYPE)
            arrived = lax.ppermute(sent, ("chip", "core"), chip_route(n_chip, n_core, stage, levels))
            summed = summed[:half] + arrived.astype(jnp.float32)
        reduced = summed[0]

        for k in range(n_ex):
            outgoing = reduced[k].astype(SUM_DTYPE)
            if k == 0:
                got[k].append(shifted(outgoing, "section", sections, 1))
            else:
                route = []
                for s in range(sections):
                    for e in range(n_ex):
                        route.append((s * n_ex + e, ((s + 1) % sections) * n_ex + (e - k) % n_ex))
                got[k].append(lax.ppermute(outgoing, ("section", "ex"), route))
    states_in = jnp.concatenate([early_in, late_in])
    outs = []
    for piece in range(pieces):
        expert_out = jnp.stack([got[k][piece] for k in range(n_ex)]).astype(jnp.float32)
        branch = jnp.einsum(
            "ect,ecd->td", selector_in, expert_out, precision=lax.Precision.HIGHEST
        )
        base = states_in[:, piece * span:(piece + 1) * span].astype(jnp.float32)
        outs.append((base + branch).astype(jnp.bfloat16))
    layer_out = jnp.concatenate(outs, axis=-1)
    return layer_out[None]


def solution(mesh):
    def run(*args):
        experts = args[5].shape[2]
        sections, ranks = mesh.devices.shape
        owners = ranks // experts
        cores = 2 if owners % 2 == 0 else 1
        devices = mesh.devices.reshape(sections, experts, owners // cores, cores)
        fine = Mesh(devices, ("section", "ex", "chip", "core"))
        dp = ("ex", "chip", "core")
        placed = (
            P("section", dp, None),
            P("section", None),
            P("section", None, dp),
            P("section", None, dp),
            P("section", dp, None),
            P("section", dp, None, None),
            P("section", dp, None),
            P("section", dp, None, None),
        )
        return jax.shard_map(
            body, mesh=fine, in_specs=placed, out_specs=P("section", dp, None), check_vma=False
        )(*args)

    return run
```

```python
import jax
import jax.numpy as jnp
from jax import lax
from jax.sharding import Mesh, PartitionSpec as P

SUM_DTYPE = jnp.bfloat16
PIECES = 2


def shifted(block, axes, size, distance):
    route = [(i, (i + distance) % size) for i in range(size)]
    return lax.ppermute(block, axes, route)


def chip_route(n_chip, n_core, stage, levels):
    route = []
    for k in range(n_chip):
        for c in range(n_core):
            bit = (stage + c) % levels
            route.append((k * n_core + c, (k ^ (1 << bit)) * n_core + c))
    return route


def body(
    hidden_states,
    norm_gain,
    gate_weight,
    up_weight,
    down_weight,
    route_rows,
    route_count,
    route_gate,
):
    states = hidden_states[0]
    scale_gain = norm_gain[0]
    gate_cols = gate_weight[0]
    up_cols = up_weight[0]
    down_rows = down_weight[0]
    slot_rows = route_rows[0, 0]
    live_count = route_count[0, 0]
    slot_gates = route_gate[0, 0]
    tok_count, width = states.shape
    experts, capacity = slot_rows.shape
    sections = lax.axis_size("section")
    n_ex = lax.axis_size("ex")
    n_chip = lax.axis_size("chip")
    n_core = lax.axis_size("core")
    levels = n_chip.bit_length() - 1
    ex_me = lax.axis_index("ex")

    live_mask = jnp.arange(capacity)[None, :] < live_count[:, None]
    weighting = jnp.where(live_mask, slot_gates, 0.0)
    selector_out = (slot_rows[..., None] == jnp.arange(tok_count)[None, None, :]).astype(
        jnp.float32
    ) * weighting[..., None]
    selector_out = jnp.roll(selector_out, -ex_me, axis=0)
    early_in = shifted(states[: tok_count // 2], "section", sections, 1)
    late_in = shifted(states[tok_count // 2 :], "section", sections, 1)
    selector_in = shifted(selector_out, "section", sections, 1)

    selector = (slot_rows.reshape(-1)[:, None] == jnp.arange(tok_count)[None, :]).astype(states.dtype)
    raw = jnp.dot(selector, states, preferred_element_type=jnp.float32).astype(states.dtype)
    raw = raw.reshape(experts, capacity, width)
    gain = scale_gain.astype(jnp.float32)

    def normalized(rows):
        rows = rows.astype(jnp.float32)
        return (
            rows * lax.rsqrt(jnp.mean(rows * rows, axis=-1, keepdims=True) + 1e-05) * gain
        ).astype(jnp.bfloat16)

    def doubled(held):
        held = held[None]
        for stage in range(levels):
            arrived = lax.ppermute(held, ("chip", "core"), chip_route(n_chip, n_core, stage, levels))
            held = jnp.concatenate([held, arrived])
        return held

    splits = 2 if capacity % 2 == 0 else 1
    chip_rows = [doubled(normalized(lax.dynamic_index_in_dim(raw, ex_me, 0, keepdims=False)))]
    for k in range(1, n_ex):
        outgoing = lax.dynamic_index_in_dim(raw, (ex_me + k) % n_ex, 0, keepdims=False)
        step = capacity // splits
        halves = []
        for h in range(splits):
            landed = shifted(outgoing[h * step:(h + 1) * step], "ex", n_ex, k)
            halves.append(doubled(normalized(landed)))
        chip_rows.append(jnp.concatenate(halves, axis=1))
    core_rows = [chip_rows] + [
        [shifted(rows, "core", n_core, q) for rows in chip_rows] for q in range(1, n_core)
    ]
    gathered = jnp.stack([jnp.stack(core_rows[q], axis=1) for q in range(n_core)])
    early_in, gathered = lax.optimization_barrier((early_in, gathered))
    flat_rows = gathered.reshape(-1, width)

    gate_part = jnp.dot(flat_rows, gate_cols, preferred_element_type=jnp.float32)
    up_part = jnp.dot(flat_rows, up_cols, preferred_element_type=jnp.float32)
    activated = (jax.nn.silu(gate_part) * up_part).astype(jnp.bfloat16)

    pieces = PIECES if width % (PIECES * 128) == 0 else 1
    span = width // pieces
    got = [[] for _ in range(n_ex)]
    for piece in range(pieces):
        cols = down_rows[:, piece * span:(piece + 1) * span]
        partial_out = jnp.dot(activated, cols, preferred_element_type=jnp.float32).astype(
            jnp.bfloat16
        )
        if piece == 0:
            late_in, selector_in, partial_out = lax.optimization_barrier(
                (late_in, selector_in, partial_out)
            )
        partials = partial_out.reshape(gathered.shape[:-1] + (span,))

        summed = partials[0].astype(jnp.float32)
        for q in range(1, n_core):
            summed = summed + shifted(partials[q], "core", n_core, -q).astype(jnp.float32)
        for stage in reversed(range(levels)):
            half = summed.shape[0] // 2
            sent = summed[half:].astype(SUM_DTYPE)
            arrived = lax.ppermute(sent, ("chip", "core"), chip_route(n_chip, n_core, stage, levels))
            summed = summed[:half] + arrived.astype(jnp.float32)
        reduced = summed[0]

        for k in range(n_ex):
            outgoing = reduced[k].astype(SUM_DTYPE)
            if k == 0:
                got[k].append(shifted(outgoing, "section", sections, 1))
            else:
                route = []
                for s in range(sections):
                    for e in range(n_ex):
                        route.append((s * n_ex + e, ((s + 1) % sections) * n_ex + (e - k) % n_ex))
                got[k].append(lax.ppermute(outgoing, ("section", "ex"), route))
    states_in = jnp.concatenate([early_in, late_in])
    outs = []
    for piece in range(pieces):
        expert_out = jnp.stack([got[k][piece] for k in range(n_ex)]).astype(jnp.float32)
        branch = jnp.einsum(
            "ect,ecd->td", selector_in, expert_out, precision=lax.Precision.HIGHEST
        )
        base = states_in[:, piece * span:(piece + 1) * span].astype(jnp.float32)
        outs.append((base + branch).astype(jnp.bfloat16))
    layer_out = jnp.concatenate(outs, axis=-1)
    return layer_out[None]


def solution(mesh):
    def run(*args):
        experts = args[5].shape[2]
        sections, ranks = mesh.devices.shape
        owners = ranks // experts
        cores = 2 if owners % 2 == 0 else 1
        devices = mesh.devices.reshape(sections, experts, owners // cores, cores)
        fine = Mesh(devices, ("section", "ex", "chip", "core"))
        dp = ("ex", "chip", "core")
        placed = (
            P("section", dp, None),
            P("section", None),
            P("section", None, dp),
            P("section", None, dp),
            P("section", dp, None),
            P("section", dp, None, None),
            P("section", dp, None),
            P("section", dp, None, None),
        )
        return jax.shard_map(
            body, mesh=fine, in_specs=placed, out_specs=P("section", dp, None), check_vma=False
        )(*args)

    return run
```
